256 devices in a mesh: gx: 16 (over y, z_lo), gy: 16 (over x, z_hi, core).
Axes of the slice: x: 4, y: 4, z: 8 (z_hi: 2, z_lo: 4; z = z_hi * 4 + z_lo), core: 2. Of those that a mesh axis runs over, the one named last changes fastest.
Arguments:
- load_vectors: float32 [16, 16, 8, 8, 192], P('gx', 'gy'), may hold values from -45 to 45
- bond_stiffness: bfloat16 [16, 16, 8, 13, 36864], P('gx', 'gy'), may hold values from 0 to 0.0016937256
- intact_words: int32 [16, 16, 8, 13, 64, 4], P('gx', 'gy'), may hold values from 0 to 65535
- block_cols: int32 [16, 16, 8, 13], P('gx', 'gy'), may hold values from 0 to 89, as said below
- self_stiffness: bfloat16 [16, 16, 8, 36864], P('gx', 'gy'), may hold values from -0.01 to 3.01, as said below
- block_inverse: float32 [16, 16, 8, 36864], P('gx', 'gy'), may hold values from -0.01 to 0.61, as said below
- coarse_basis: float32 [16, 16, 16, 8, 192], P('gx', 'gy'), may hold values from -0.3 to 0.3
- coarse_factor: float32 [4096, 4096], P(('gx', 'gy')), may hold values from -0.375 to 0.375
Outputs:
- displacement: float32 [16, 16, 8, 8, 192], P('gx', 'gy')
- residual: float32 [16, 16, 8, 8, 192], P('gx', 'gy')
The draws below stay inside these ranges and needn't reach their ends.
Inputs may be any that keep to these rules, and one draw needn't show every extreme that they name: `block_cols`: the 13 codes of a block name different blocks among the 26 around it (never the block itself), each |a - 1|, |c - 1|, |w - 1 - z| at most 1. `self_stiffness`: each block, read as a matrix, is symmetric. `block_inverse`: each block, read as a matrix, is symmetric.
All inputs are finite; a program needn't handle non-finite values.
Results may differ from the reference program's by a relative error of at most 0.0055.
Values may be sent and summed in bfloat16 or wider, within the bound.
No kernel may reach another device: no remote copies, remote signals or barrier semaphores. Data moves between devices by JAX's collectives and lax.ppermute only.
A program may use at most 128 MiB of HBM per device.

```python
import math
import jax
import jax.numpy as jnp
from jax import lax

COMP = 3
PB = 64
DOF = 192
WORDS = 4
NS = 13
BZ = 8
NLOAD = 8
CVD = 16
ITERS = 2
NBX = 16
NBY = 16
CV = 4096


def draw_load_vectors(key, part):
    shape = (NBX, NBY, BZ, NLOAD, DOF)
    order = jnp.arange(NBX, dtype=jnp.float32)[:, None] * NBY + jnp.arange(NBY, dtype=jnp.float32)[None, :]
    fraction = order / max(NBX * NBY - 1, 1)
    key_one = jax.random.fold_in(key, 0)
    growth = 3.0 ** (0.5 * fraction)
    sample = jnp.clip(jax.random.normal(key_one, shape, jnp.float32), -5.0, 5.0) + 0.6
    return sample * growth[:, :, None, None, None]


def symmetric_blocks(key, spread, lower, upper):
    key_one, key_two = jax.random.split(key)
    shape = (NBX, NBY, BZ, DOF, DOF)
    noise = jax.random.uniform(key_one, shape, jnp.float32, -1.0, 1.0) * (spread / DOF)
    paired = noise + jnp.swapaxes(noise, -1, -2)
    middle = jnp.exp(jax.random.uniform(key_two, (NBX, NBY, BZ, DOF), jnp.float32, math.log(lower), math.log(upper)))
    full = paired + jnp.eye(DOF, dtype=jnp.float32) * middle[..., None, :]
    return full.reshape(NBX, NBY, BZ, DOF * DOF)


def draw_self_stiffness(key, part):
    return symmetric_blocks(jax.random.fold_in(key, 11), 0.3, 1.0, 3.0).astype(jnp.bfloat16)


def draw_block_inverse(key, part):
    return symmetric_blocks(jax.random.fold_in(key, 23), 0.08, 0.2, 0.6)


def draw_block_cols(key, part):
    count = NBX * NBY * BZ
    subkeys = jax.random.split(jax.random.fold_in(key, 37), count)
    orders = jax.vmap(lambda single: jax.random.permutation(single, 26))(subkeys)
    chosen = orders[:, :NS].astype(jnp.int32)
    beside_all = chosen + (chosen >= 13).astype(jnp.int32)
    height = (jnp.arange(count, dtype=jnp.int32) % BZ)[:, None]
    depth_span = BZ + 2
    codes = beside_all // 9 * (3 * depth_span) + beside_all // 3 % 3 * depth_span + height + beside_all % 3
    return codes.reshape(NBX, NBY, BZ, NS).astype(jnp.int32)


def touch_ends(values, key, low, top_value):
    index_at = [jax.random.randint(jax.random.fold_in(key, axis), (), 0, length) for axis, length in enumerate(values.shape)]
    widest = values.shape.index(max(values.shape))
    neighbour = index_at[:widest] + [(index_at[widest] + 1) % values.shape[widest]] + index_at[widest + 1:]
    return values.at[tuple(index_at)].set(low).at[tuple(neighbour)].set(top_value)


def with_spikes(array, stream_key, source, target, parts, factor):
    owner, partner = [(jnp.arange(array.shape[position]) // (array.shape[position] // parts)).reshape([-1 if axis == position else 1 for axis in range(array.ndim)]) for position in (source, target)]
    chosen = jax.random.permutation(stream_key, parts)[partner]
    strong = (owner == chosen) | (owner == (partner + parts // 2) % parts)
    return jnp.where(strong, factor * array, array)


def steps_of(own_key, dims, cuts, least, high):
    loudness = 1.0
    for dim, shards_of in cuts:
        draws = jax.random.uniform(jax.random.fold_in(jax.random.fold_in(own_key, 6), dim), (shards_of,), jnp.float32, least / len(cuts), high / len(cuts))
        loudness = loudness * jnp.repeat(jnp.exp(draws), dims[dim] // shards_of).reshape((-1,) + (1,) * (len(dims) - 1 - dim))
    return loudness


def gaussian(key, extent, width, reach, shards=(), held_as=jnp.bfloat16):
    drawn = width * jax.random.normal(key, extent, jnp.float32)
    if shards:
        drawn = drawn * steps_of(key, extent, shards, -0.22, 0.18)
    return jnp.clip(drawn, -reach, reach).astype(held_as)


def gaussian_with(rng, shape, deviation, reach, cuts, heavy, kind=jnp.bfloat16):
    result = deviation * jax.random.normal(rng, shape, jnp.float32)
    if cuts:
        result = result * steps_of(rng, shape, cuts, -0.22, 0.18)
    return jnp.clip(with_spikes(result, jax.random.fold_in(rng, 3), *heavy), -reach, reach).astype(kind)


def setup_inputs(seed: int = 0) -> dict:
    streams_of = jax.random.split(jax.random.key(seed), 9)
    load_vectors = draw_load_vectors(jax.random.fold_in(streams_of[8], 71), 0)
    bond_stiffness = jnp.clip(0.0016937256 * jax.random.uniform(streams_of[1], (NBX, NBY, BZ, NS, DOF * DOF), jnp.float32) ** steps_of(streams_of[1], (NBX, NBY, BZ, NS, DOF * DOF), ((0, 16), (1, 16)), -0.2, 0.2), 0.0, 0.0016937256).astype(jnp.bfloat16)
    intact_words = touch_ends(jax.random.randint(streams_of[2], (NBX, NBY, BZ, NS, PB, WORDS), 0, 65536), jax.random.fold_in(streams_of[2], 1), 0, 65535).astype(jnp.int32)
    block_cols = draw_block_cols(jax.random.fold_in(streams_of[8], 71), 0)
    self_stiffness = draw_self_stiffness(jax.random.fold_in(streams_of[8], 71), 0)
    block_inverse = draw_block_inverse(jax.random.fold_in(streams_of[8], 71), 0)
    coarse_basis = gaussian(streams_of[6], (NBX, NBY, CVD, BZ, DOF), 0.05, 0.3, ((0, 16), (1, 16)), jnp.float32)
    coarse_factor = gaussian_with(streams_of[7], (CV, CV), CV ** -0.5, 0.375, ((0, 256),), (0, 1, 256, 6.0), jnp.float32)
    return dict(load_vectors=load_vectors, bond_stiffness=bond_stiffness, intact_words=intact_words, block_cols=block_cols, self_stiffness=self_stiffness, block_inverse=block_inverse, coarse_basis=coarse_basis, coarse_factor=coarse_factor)


highest = lax.Precision.HIGHEST


def unpack_bits(packed):
    shifts = jnp.arange(16, dtype=jnp.int32)
    bitset = jnp.right_shift(packed[..., None], shifts) & 1
    return bitset.reshape(packed.shape[:-1] + (packed.shape[-1] * 16,))


def masked_blocks(stiffness, packed):
    intact = unpack_bits(packed).astype(stiffness.dtype)
    leading = stiffness.shape[:-1]
    shaped = stiffness.reshape(leading + (COMP, PB, COMP, PB))
    masked = shaped * intact[..., None, :, None, :]
    return masked.reshape(leading + (DOF, DOF))


def decode_cols(block_cols):
    depth_span = BZ + 2
    return block_cols // (3 * depth_span), (block_cols // depth_span) % 3, block_cols % depth_span


def apply_operator(vector_in, bond_stiffness, intact_words, block_cols, self_stiffness):
    padded = jnp.pad(vector_in, ((1, 1), (1, 1), (1, 1), (0, 0), (0, 0)))
    shift_rows, shift_cols, depth_idx = decode_cols(block_cols)
    across = jnp.arange(NBY, dtype=jnp.int32)[:, None, None]

    def one_row(row_items):
        row_index, stiff_row, packed_row, rows_r, cols_r, depth_r, self_row = row_items
        weights = masked_blocks(stiff_row, packed_row).astype(jnp.float32)
        own_part = vector_in[row_index].astype(jnp.float32)
        ghosts = padded[row_index + rows_r, across + cols_r, depth_r].astype(jnp.float32)
        row_total = jnp.sum(weights, axis=(2, 4))
        column_total = jnp.sum(weights, axis=3)
        forward = row_total[:, :, None, :] * own_part - jnp.einsum('ybsij,ybslj->ybli', weights, ghosts, precision=highest)
        backward = column_total[:, :, :, None, :] * ghosts - jnp.einsum('ybsij,ybli->ybslj', weights, own_part, precision=highest)
        self_matrix = self_row.reshape(NBY, BZ, DOF, DOF).astype(jnp.float32)
        diagonal = jnp.einsum('ybij,yblj->ybli', self_matrix, own_part, precision=highest)
        return forward + diagonal, backward

    rows_out, partial_value = lax.map(one_row, (jnp.arange(NBX, dtype=jnp.int32), bond_stiffness, intact_words, shift_rows, shift_cols, depth_idx, self_stiffness))
    target_rows = jnp.arange(NBX, dtype=jnp.int32)[:, None, None, None] + shift_rows
    target_cols = jnp.arange(NBY, dtype=jnp.int32)[None, :, None, None] + shift_cols
    pooled = jnp.zeros((NBX + 2, NBY + 2, BZ + 2, NLOAD, DOF), jnp.float32)
    pooled = pooled.at[target_rows, target_cols, depth_idx].add(partial_value)
    return rows_out + pooled[1:-1, 1:-1, 1:-1]


def precondition(residual, block_inverse, coarse_basis, coarse_factor):
    inverse = block_inverse.reshape(NBX, NBY, BZ, DOF, DOF)
    own_part = jnp.einsum('xybij,xyblj->xybli', inverse, residual, precision=highest)
    restricted = jnp.einsum('xykbi,xybli->lxyk', coarse_basis, residual, precision=highest).reshape(NLOAD, CV)
    summed = jnp.dot(restricted, coarse_factor, precision=highest)
    spread = jnp.dot(summed, coarse_factor.T, precision=highest).reshape(NLOAD, NBX, NBY, CVD)
    return own_part + jnp.einsum('xykbi,lxyk->xybli', coarse_basis, spread, precision=highest)


def reference(load_vectors, bond_stiffness, intact_words, block_cols, self_stiffness, block_inverse, coarse_basis, coarse_factor):
    solution = jnp.zeros_like(load_vectors)
    residual = load_vectors
    smoothed = precondition(residual, block_inverse, coarse_basis, coarse_factor)
    direction = smoothed
    energy = jnp.sum(residual * smoothed, axis=(0, 1, 2, 4))
    for iteration in range(ITERS):
        rounded = lax.optimization_barrier(direction.astype(jnp.bfloat16))
        operator_out = apply_operator(rounded, bond_stiffness, intact_words, block_cols, self_stiffness)
        step_size = energy / jnp.sum(direction * operator_out, axis=(0, 1, 2, 4))
        step_scale = step_size[None, None, None, :, None]
        solution = solution + step_scale * direction
        residual = residual - step_scale * operator_out
        if iteration + 1 < ITERS:
            smoothed = precondition(residual, block_inverse, coarse_basis, coarse_factor)
            new_energy = jnp.sum(residual * smoothed, axis=(0, 1, 2, 4))
            direction = smoothed + (new_energy / energy)[None, None, None, :, None] * direction
            energy = new_energy
    return solution, residual
```

```python
import jax
import jax.numpy as jnp
from jax import lax
from jax.sharding import PartitionSpec as P

COMP = 3
PB = 64
DOF = 192
NS = 13
BZ = 8
NLOAD = 8
ITERS = 2


highest = lax.Precision.HIGHEST


def all_sum(x):
    for axis in ("gy", "gx"):
        size = lax.axis_size(axis)
        if size & (size - 1):
            x = lax.psum(x, axis)
            continue
        span = 1
        while span < size:
            pairs = [(i, i ^ span) for i in range(size)]
            x = x + lax.ppermute(x, axis, pairs)
            span *= 2
    return x


def padded_2(x, sides, width):
    for axis, dim in sides:
        size, length = (lax.axis_size(axis), x.shape[dim])
        up = [(i, (i + 1) % size) for i in range(size - 1)]
        down = [(j, i) for i, j in up]
        last = lax.slice_in_dim(x, length - width, length, axis=dim)
        initial = lax.slice_in_dim(x, 0, width, axis=dim)
        before = lax.ppermute(last, axis, up)
        after = lax.ppermute(initial, axis, down)
        x = jnp.concatenate([before, x, after], axis=dim)
    return x


def unpack_bits(packed):
    shifts = jnp.arange(16, dtype=jnp.int32)
    bitset = jnp.right_shift(packed[..., None], shifts) & 1
    return bitset.reshape(packed.shape[:-1] + (packed.shape[-1] * 16,))


def masked_blocks(stiffness, packed):
    intact = unpack_bits(packed).astype(stiffness.dtype)
    leading = stiffness.shape[:-1]
    shaped = stiffness.reshape(leading + (COMP, PB, COMP, PB))
    masked = shaped * intact[..., None, :, None, :]
    return masked.reshape(leading + (DOF, DOF))


def per_device(
    load_vectors,
    bond_stiffness,
    intact_words,
    block_cols,
    self_stiffness,
    block_inverse,
    coarse_basis,
    coarse_factor,
):
    weights = masked_blocks(bond_stiffness[0, 0], intact_words[0, 0])
    row_total = jnp.sum(weights, axis=(1, 3), dtype=jnp.float32)
    column_total = jnp.sum(weights, axis=2, dtype=jnp.float32)
    col_codes = block_cols[0, 0]
    depth_span = BZ + 2
    ghost_count = 9 * depth_span
    selector = (
        jnp.arange(ghost_count, dtype=jnp.int32)[:, None] == col_codes.reshape(-1)[None, :]
    ).astype(jnp.bfloat16)
    self_block = self_stiffness[0, 0].reshape(BZ, DOF, DOF)
    inverse = block_inverse[0, 0].reshape(BZ, DOF, DOF)
    coarse_vecs = coarse_basis[0, 0]

    def precondition(residual):
        own_part = jnp.einsum("bij,blj->bli", inverse, residual, precision=highest)
        restricted = jnp.einsum("kbi,bli->lk", coarse_vecs, residual, precision=highest)
        coarse_term = jnp.dot(restricted, coarse_factor, precision=highest)
        local_energy = jnp.sum(residual * own_part, axis=(0, 2))
        summed = all_sum(jnp.concatenate([coarse_term, local_energy[:, None]], axis=1))
        coarse_sum = summed[:, :-1]
        spread = jnp.einsum("lc,kc->lk", coarse_sum, coarse_factor, precision=highest)
        smoothed = own_part + jnp.einsum("kbi,lk->bli", coarse_vecs, spread, precision=highest)
        energy = summed[:, -1] + jnp.sum(coarse_sum * coarse_sum, axis=1)
        return (smoothed, energy)

    residual = load_vectors[0, 0]
    solution = jnp.zeros_like(residual)
    smoothed, energy = precondition(residual)
    direction = smoothed
    for iteration in range(ITERS):
        rounded = direction.astype(jnp.bfloat16)
        ghosts = padded_2(rounded[None, None], (("gx", 0), ("gy", 1)), 1)
        padded = jnp.pad(ghosts, ((0, 0), (0, 0), (1, 1), (0, 0), (0, 0))).reshape(
            ghost_count, NLOAD, DOF
        )
        gathered = jnp.take(padded, col_codes, axis=0)
        forward = row_total[:, None, :] * rounded - jnp.einsum(
            "bsij,bslj->bli", weights, gathered, preferred_element_type=jnp.float32
        )
        backward = column_total[:, :, None, :] * gathered - jnp.einsum(
            "bsij,bli->bslj", weights, rounded, preferred_element_type=jnp.float32
        )
        flat_terms = backward.reshape(BZ * NS, NLOAD * DOF)
        high_part = flat_terms.astype(jnp.bfloat16)
        low_part = (flat_terms - high_part.astype(jnp.float32)).astype(jnp.bfloat16)
        apply_spread = jnp.dot(selector, high_part, preferred_element_type=jnp.float32) + jnp.dot(
            selector, low_part, preferred_element_type=jnp.float32
        )
        partial_value = apply_spread.reshape(3, 3, depth_span, NLOAD, DOF)[:, :, 1 : depth_span - 1]
        beside_all = padded_2(partial_value.astype(jnp.bfloat16), (("gx", 0), ("gy", 1)), 1).astype(
            partial_value.dtype
        )
        folded = (
            beside_all[2, 2]
            + beside_all[0, 0]
            + beside_all[0, 2]
            + beside_all[0, 4]
            + beside_all[2, 0]
        )
        folded = folded + beside_all[2, 4] + beside_all[4, 0] + beside_all[4, 2] + beside_all[4, 4]
        diagonal = jnp.einsum(
            "bij,blj->bli", self_block, rounded, preferred_element_type=jnp.float32
        )
        operator_out = diagonal + forward + folded
        curve_sum = all_sum(jnp.sum(direction * operator_out, axis=(0, 2)))
        step_scale = (energy / curve_sum)[None, :, None]
        solution = solution + step_scale * direction
        residual = residual - step_scale * operator_out
        if iteration + 1 < ITERS:
            smoothed, new_energy = precondition(residual)
            direction = smoothed + (new_energy / energy)[None, :, None] * direction
            energy = new_energy
    return (solution[None, None], residual[None, None])


def solution(mesh):
    in_specs = (
        P("gx", "gy", None, None, None),
        P("gx", "gy", None, None, None),
        P("gx", "gy", None, None, None, None),
        P("gx", "gy", None, None),
        P("gx", "gy", None, None),
        P("gx", "gy", None, None),
        P("gx", "gy", None, None, None),
        P(("gx", "gy"), None),
    )
    out_specs = (P("gx", "gy", None, None, None), P("gx", "gy", None, None, None))
    return jax.shard_map(
        per_device, mesh=mesh, in_specs=in_specs, out_specs=out_specs, check_vma=False
    )
```

```python
import jax
import jax.numpy as jnp
from jax import lax
from jax.sharding import PartitionSpec as P

COMP = 3
PB = 64
DOF = 192
NS = 13
BZ = 8
NLOAD = 8
ITERS = 2


highest = lax.Precision.HIGHEST


def all_sum(x):
    for axis in ("gy", "gx"):
        size = lax.axis_size(axis)
        if size & (size - 1):
            x = lax.psum(x, axis)
            continue
        span = 1
        while span < size:
            pairs = [(i, i ^ span) for i in range(size)]
            x = x + lax.ppermute(x, axis, pairs)
            span *= 2
    return x


def padded_2(x, sides, width):
    for axis, dim in sides:
        size, length = (lax.axis_size(axis), x.shape[dim])
        up = [(i, (i + 1) % size) for i in range(size - 1)]
        down = [(j, i) for i, j in up]
        last = lax.slice_in_dim(x, length - width, length, axis=dim)
        initial = lax.slice_in_dim(x, 0, width, axis=dim)
        before = lax.ppermute(last, axis, up)
        after = lax.ppermute(initial, axis, down)
        x = jnp.concatenate([before, x, after], axis=dim)
    return x


def unpack_bits(packed):
    shifts = jnp.arange(16, dtype=jnp.int32)
    bitset = jnp.right_shift(packed[..., None], shifts) & 1
    return bitset.reshape(packed.shape[:-1] + (packed.shape[-1] * 16,))


def masked_blocks(stiffness, packed):
    intact = unpack_bits(packed).astype(stiffness.dtype)
    leading = stiffness.shape[:-1]
    spread = (
        jnp.arange(DOF, dtype=jnp.int32)[:, None] % PB == jnp.arange(PB, dtype=jnp.int32)[None, :]
    ).astype(stiffness.dtype)
    wide = jnp.einsum("Ii,...ij,Jj->...IJ", spread, intact, spread, preferred_element_type=jnp.float32)
    return stiffness.reshape(leading + (DOF, DOF)) * wide.astype(stiffness.dtype)


def per_device(
    load_vectors,
    bond_stiffness,
    intact_words,
    block_cols,
    self_stiffness,
    block_inverse,
    coarse_basis,
    coarse_factor,
):
    weights = masked_blocks(bond_stiffness[0, 0], intact_words[0, 0])
    row_total = jnp.sum(weights, axis=(1, 3), dtype=jnp.float32)
    column_total = jnp.sum(weights, axis=2, dtype=jnp.float32)
    col_codes = block_cols[0, 0]
    depth_span = BZ + 2
    ghost_count = 9 * depth_span
    selector = (
        jnp.arange(ghost_count, dtype=jnp.int32)[:, None] == col_codes.reshape(-1)[None, :]
    ).astype(jnp.bfloat16)
    self_block = self_stiffness[0, 0].reshape(BZ, DOF, DOF)
    inverse = block_inverse[0, 0].reshape(BZ, DOF, DOF)
    coarse_vecs = coarse_basis[0, 0]

    def precondition(residual):
        own_part = jnp.einsum("bij,blj->bli", inverse, residual, precision=highest)
        restricted = jnp.einsum("kbi,bli->lk", coarse_vecs, residual, precision=highest)
        coarse_term = jnp.dot(restricted, coarse_factor, precision=highest)
        local_energy = jnp.sum(residual * own_part, axis=(0, 2))
        summed = all_sum(jnp.concatenate([coarse_term, local_energy[:, None]], axis=1))
        coarse_sum = summed[:, :-1]
        spread = jnp.einsum("lc,kc->lk", coarse_sum, coarse_factor, precision=highest)
        smoothed = own_part + jnp.einsum("kbi,lk->bli", coarse_vecs, spread, precision=highest)
        energy = summed[:, -1] + jnp.sum(coarse_sum * coarse_sum, axis=1)
        return (smoothed, energy)

    residual = load_vectors[0, 0]
    solution = jnp.zeros_like(residual)
    smoothed, energy = precondition(residual)
    direction = smoothed
    for iteration in range(ITERS):
        rounded = direction.astype(jnp.bfloat16)
        ghosts = padded_2(rounded[None, None], (("gx", 0), ("gy", 1)), 1)
        padded = jnp.pad(ghosts, ((0, 0), (0, 0), (1, 1), (0, 0), (0, 0))).reshape(
            ghost_count, NLOAD, DOF
        )
        gathered = jnp.take(padded, col_codes, axis=0)
        forward = row_total[:, None, :] * rounded - jnp.einsum(
            "bsij,bslj->bli", weights, gathered, preferred_element_type=jnp.float32
        )
        backward = column_total[:, :, None, :] * gathered - jnp.einsum(
            "bsij,bli->bslj", weights, rounded, preferred_element_type=jnp.float32
        )
        flat_terms = backward.reshape(BZ * NS, NLOAD * DOF)
        high_part = flat_terms.astype(jnp.bfloat16)
        low_part = (flat_terms - high_part.astype(jnp.float32)).astype(jnp.bfloat16)
        apply_spread = jnp.dot(selector, high_part, preferred_element_type=jnp.float32) + jnp.dot(
            selector, low_part, preferred_element_type=jnp.float32
        )
        partial_value = apply_spread.reshape(3, 3, depth_span, NLOAD, DOF)[:, :, 1 : depth_span - 1]
        beside_all = padded_2(partial_value.astype(jnp.bfloat16), (("gx", 0), ("gy", 1)), 1).astype(
            partial_value.dtype
        )
        folded = (
            beside_all[2, 2]
            + beside_all[0, 0]
            + beside_all[0, 2]
            + beside_all[0, 4]
            + beside_all[2, 0]
        )
        folded = folded + beside_all[2, 4] + beside_all[4, 0] + beside_all[4, 2] + beside_all[4, 4]
        diagonal = jnp.einsum(
            "bij,blj->bli", self_block, rounded, preferred_element_type=jnp.float32
        )
        operator_out = diagonal + forward + folded
        curve_sum = all_sum(jnp.sum(direction * operator_out, axis=(0, 2)))
        step_scale = (energy / curve_sum)[None, :, None]
        solution = solution + step_scale * direction
        residual = residual - step_scale * operator_out
        if iteration + 1 < ITERS:
            smoothed, new_energy = precondition(residual)
            direction = smoothed + (new_energy / energy)[None, :, None] * direction
            energy = new_energy
    return (solution[None, None], residual[None, None])


def solution(mesh):
    in_specs = (
        P("gx", "gy", None, None, None),
        P("gx", "gy", None, None, None),
        P("gx", "gy", None, None, None, None),
        P("gx", "gy", None, None),
        P("gx", "gy", None, None),
        P("gx", "gy", None, None),
        P("gx", "gy", None, None, None),
        P(("gx", "gy"), None),
    )
    out_specs = (P("gx", "gy", None, None, None), P("gx", "gy", None, None, None))
    return jax.shard_map(
        per_device, mesh=mesh, in_specs=in_specs, out_specs=out_specs, check_vma=False
    )
```

```python
import jax
import jax.numpy as jnp
from jax import lax
from jax.sharding import PartitionSpec as P

COMP = 3
PB = 64
DOF = 192
NS = 13
BZ = 8
NLOAD = 8
ITERS = 2


highest = lax.Precision.HIGHEST


def all_sum(x):
    for axis in ("gy", "gx"):
        size = lax.axis_size(axis)
        if size & (size - 1):
            x = lax.psum(x, axis)
            continue
        span = 1
        while span < size:
            pairs = [(i, i ^ span) for i in range(size)]
            x = x + lax.ppermute(x, axis, pairs)
            span *= 2
    return x


def unpack_bits(packed):
    shifts = jnp.arange(16, dtype=jnp.int32)
    bitset = jnp.right_shift(packed[..., None], shifts) & 1
    return bitset.reshape(packed.shape[:-1] + (packed.shape[-1] * 16,))


def masked_blocks(stiffness, packed):
    intact = unpack_bits(packed).astype(stiffness.dtype)
    leading = stiffness.shape[:-1]
    spread = (
        jnp.arange(DOF, dtype=jnp.int32)[:, None] % PB == jnp.arange(PB, dtype=jnp.int32)[None, :]
    ).astype(stiffness.dtype)
    wide = jnp.einsum("Ii,...ij,Jj->...IJ", spread, intact, spread, preferred_element_type=jnp.float32)
    return stiffness.reshape(leading + (DOF, DOF)) * wide.astype(stiffness.dtype)


def neighbour_swap(parts, mesh_shape):
    nx, ny = mesh_shape
    arrived = {}
    for (a, c), value in parts.items():
        dx, dy = a - 1, c - 1
        pairs = [
            (i * ny + j, (i + dx) * ny + (j + dy))
            for i in range(nx)
            for j in range(ny)
            if 0 <= i + dx < nx and 0 <= j + dy < ny
        ]
        arrived[(2 - a, 2 - c)] = lax.ppermute(value, ("gx", "gy"), pairs)
    return arrived


def per_device(
    load_vectors,
    bond_stiffness,
    intact_words,
    block_cols,
    self_stiffness,
    block_inverse,
    coarse_basis,
    coarse_factor,
):
    mesh_shape = (lax.axis_size("gx"), lax.axis_size("gy"))
    sides = [(a, c) for a in range(3) for c in range(3) if (a, c) != (1, 1)]
    weights = masked_blocks(bond_stiffness[0, 0], intact_words[0, 0])
    row_total = jnp.sum(weights, axis=(1, 3), dtype=jnp.float32)
    column_total = jnp.sum(weights, axis=2, dtype=jnp.float32)
    col_codes = block_cols[0, 0]
    depth_span = BZ + 2
    ghost_count = 9 * depth_span
    selector = (
        jnp.arange(ghost_count, dtype=jnp.int32)[:, None] == col_codes.reshape(-1)[None, :]
    ).astype(jnp.bfloat16)
    self_block = self_stiffness[0, 0].reshape(BZ, DOF, DOF)
    inverse = block_inverse[0, 0].reshape(BZ, DOF, DOF)
    coarse_vecs = coarse_basis[0, 0]

    def spread_terms(flat_terms, tail):
        high_part = flat_terms.astype(jnp.bfloat16)
        low_part = (flat_terms - high_part.astype(jnp.float32)).astype(jnp.bfloat16)
        spread = jnp.dot(selector, high_part, preferred_element_type=jnp.float32) + jnp.dot(
            selector, low_part, preferred_element_type=jnp.float32
        )
        return spread.reshape((3, 3, depth_span) + tail)[:, :, 1 : depth_span - 1]

    column_spread = spread_terms(column_total.reshape(BZ * NS, DOF), (DOF,))
    column_in = neighbour_swap({side: column_spread[side] for side in sides}, mesh_shape)
    column_fold = column_spread[1, 1]
    for side in sides:
        column_fold = column_fold + column_in[side]

    def precondition(residual):
        own_part = jnp.einsum("bij,blj->bli", inverse, residual, precision=highest)
        restricted = jnp.einsum("kbi,bli->lk", coarse_vecs, residual, precision=highest)
        coarse_term = jnp.dot(restricted, coarse_factor, precision=highest)
        local_energy = jnp.sum(residual * own_part, axis=(0, 2))
        summed = all_sum(jnp.concatenate([coarse_term, local_energy[:, None]], axis=1))
        coarse_sum = summed[:, :-1]
        spread = jnp.einsum("lc,kc->lk", coarse_sum, coarse_factor, precision=highest)
        smoothed = own_part + jnp.einsum("kbi,lk->bli", coarse_vecs, spread, precision=highest)
        energy = summed[:, -1] + jnp.sum(coarse_sum * coarse_sum, axis=1)
        return (smoothed, energy)

    residual = load_vectors[0, 0]
    solution = jnp.zeros_like(residual)
    smoothed, energy = precondition(residual)
    direction = smoothed
    for iteration in range(ITERS):
        rounded = direction.astype(jnp.bfloat16)
        backward = -jnp.einsum("bsij,bli->bslj", weights, rounded, preferred_element_type=jnp.float32)
        partial_value = spread_terms(backward.reshape(BZ * NS, NLOAD * DOF), (NLOAD, DOF))
        high = partial_value.astype(jnp.bfloat16)
        low = (partial_value - high.astype(jnp.float32)).astype(jnp.bfloat16)
        outgoing = {side: jnp.stack([rounded, high[side], low[side]]) for side in sides}
        arrived = neighbour_swap(outgoing, mesh_shape)
        ghost_rows = []
        for a in range(3):
            for c in range(3):
                ghost_rows.append(rounded if (a, c) == (1, 1) else arrived[(a, c)][0])
        ghosts = jnp.stack(ghost_rows).reshape(3, 3, BZ, NLOAD, DOF)
        padded = jnp.pad(ghosts, ((0, 0), (0, 0), (1, 1), (0, 0), (0, 0))).reshape(
            ghost_count, NLOAD, DOF
        )
        gathered = jnp.take(padded, col_codes, axis=0)
        forward = row_total[:, None, :] * rounded - jnp.einsum(
            "bsij,bslj->bli", weights, gathered, preferred_element_type=jnp.float32
        )
        folded = partial_value[1, 1]
        for side in sides:
            got = arrived[side]
            folded = folded + (got[1].astype(jnp.float32) + got[2].astype(jnp.float32))
        folded = folded + column_fold[:, None, :] * rounded.astype(jnp.float32)
        diagonal = jnp.einsum(
            "bij,blj->bli", self_block, rounded, preferred_element_type=jnp.float32
        )
        operator_out = diagonal + forward + folded
        curve_sum = all_sum(jnp.sum(direction * operator_out, axis=(0, 2)))
        step_scale = (energy / curve_sum)[None, :, None]
        solution = solution + step_scale * direction
        residual = residual - step_scale * operator_out
        if iteration + 1 < ITERS:
            smoothed, new_energy = precondition(residual)
            direction = smoothed + (new_energy / energy)[None, :, None] * direction
            energy = new_energy
    return (solution[None, None], residual[None, None])


def solution(mesh):
    in_specs = (
        P("gx", "gy", None, None, None),
        P("gx", "gy", None, None, None),
        P("gx", "gy", None, None, None, None),
        P("gx", "gy", None, None),
        P("gx", "gy", None, None),
        P("gx", "gy", None, None),
        P("gx", "gy", None, None, None),
        P(("gx", "gy"), None),
    )
    out_specs = (P("gx", "gy", None, None, None), P("gx", "gy", None, None, None))
    return jax.shard_map(
        per_device, mesh=mesh, in_specs=in_specs, out_specs=out_specs, check_vma=False
    )
```

```python
import jax
import jax.numpy as jnp
from jax import lax
from jax.sharding import PartitionSpec as P

COMP = 3
PB = 64
DOF = 192
NS = 13
BZ = 8
NLOAD = 8
ITERS = 2


highest = lax.Precision.HIGHEST


def all_sum(x, radix=2):
    for axis in ("gy", "gx"):
        size = lax.axis_size(axis)
        if size & (size - 1):
            x = lax.psum(x, axis)
            continue
        span = 1
        while span < size:
            count = min(radix, size // span)
            values = [x] + [
                lax.ppermute(x, axis, [(i, i ^ (o * span)) for i in range(size)])
                for o in range(1, count)
            ]
            width = 1
            while width < count:
                values = [
                    values[o] + values[o + width] if o % (2 * width) == 0 else None
                    for o in range(count)
                ]
                width *= 2
            x = values[0]
            span *= count
    return x


def shift_pairs(size):
    up = [(i, i + 1) for i in range(size - 1)]
    return up, [(j, i) for i, j in up]


def fold_in(part):
    up, down = shift_pairs(lax.axis_size("gx"))
    from_left = lax.ppermute(part[2], "gx", up)
    from_right = lax.ppermute(part[0], "gx", down)
    here_x = jnp.stack([from_left, part[1], from_right])
    up, down = shift_pairs(lax.axis_size("gy"))
    from_below = lax.ppermute(here_x[:, 2], "gy", up)
    from_above = lax.ppermute(here_x[:, 0], "gy", down)
    return jnp.sum(here_x[:, 1], axis=0) + jnp.sum(from_below, axis=0) + jnp.sum(from_above, axis=0)


def exchange(rounded, part, own_part):
    up, down = shift_pairs(lax.axis_size("gx"))
    from_left = lax.ppermute(jnp.concatenate([rounded[None], part[2]]), "gx", up)
    from_right = lax.ppermute(jnp.concatenate([rounded[None], part[0]]), "gx", down)
    ghost_x = jnp.stack([from_left[0], rounded, from_right[0]])
    part_x = jnp.stack([from_left[1:], part[1], from_right[1:]])
    up, down = shift_pairs(lax.axis_size("gy"))
    from_below = lax.ppermute(jnp.concatenate([ghost_x, part_x[:, 2]]), "gy", up)
    from_above = lax.ppermute(jnp.concatenate([ghost_x, part_x[:, 0]]), "gy", down)
    ghosts = jnp.stack([from_below[:3], ghost_x, from_above[:3]], axis=1)
    wide = jnp.float32
    folded = own_part + from_left[2].astype(wide) + from_right[2].astype(wide)
    folded = folded + jnp.sum(from_below[3:].astype(wide), axis=0)
    folded = folded + jnp.sum(from_above[3:].astype(wide), axis=0)
    return ghosts, folded


def unpack_bits(packed):
    shifts = jnp.arange(16, dtype=jnp.int32)
    bitset = jnp.right_shift(packed[..., None], shifts) & 1
    return bitset.reshape(packed.shape[:-1] + (packed.shape[-1] * 16,))


def masked_blocks(stiffness, packed):
    intact = unpack_bits(packed).astype(stiffness.dtype)
    leading = stiffness.shape[:-1]
    spread = (
        jnp.arange(DOF, dtype=jnp.int32)[:, None] % PB == jnp.arange(PB, dtype=jnp.int32)[None, :]
    ).astype(stiffness.dtype)
    wide = jnp.einsum("Ii,...ij,Jj->...IJ", spread, intact, spread, preferred_element_type=jnp.float32)
    return stiffness.reshape(leading + (DOF, DOF)) * wide.astype(stiffness.dtype)


def per_device(
    load_vectors,
    bond_stiffness,
    intact_words,
    block_cols,
    self_stiffness,
    block_inverse,
    coarse_basis,
    coarse_factor,
):
    weights = masked_blocks(bond_stiffness[0, 0], intact_words[0, 0])
    row_total = jnp.sum(weights, axis=(1, 3), dtype=jnp.float32)
    column_total = jnp.sum(weights, axis=2, dtype=jnp.float32)
    col_codes = block_cols[0, 0]
    depth_span = BZ + 2
    ghost_count = 9 * depth_span
    selector = (
        jnp.arange(ghost_count, dtype=jnp.int32)[:, None] == col_codes.reshape(-1)[None, :]
    ).astype(jnp.bfloat16)
    self_block = self_stiffness[0, 0].reshape(BZ, DOF, DOF)
    inverse = block_inverse[0, 0].reshape(BZ, DOF, DOF)
    coarse_vecs = coarse_basis[0, 0]

    def spread_terms(flat_terms, tail):
        high_part = flat_terms.astype(jnp.bfloat16)
        low_part = (flat_terms - high_part.astype(jnp.float32)).astype(jnp.bfloat16)
        spread = jnp.dot(selector, high_part, preferred_element_type=jnp.float32) + jnp.dot(
            selector, low_part, preferred_element_type=jnp.float32
        )
        return spread.reshape((3, 3, depth_span) + tail)[:, :, 1 : depth_span - 1]

    column_spread = spread_terms(column_total.reshape(BZ * NS, DOF), (DOF,))
    column_fold = fold_in(column_spread)

    def precondition(residual):
        own_part = jnp.einsum("bij,blj->bli", inverse, residual, precision=highest)
        restricted = jnp.einsum("kbi,bli->lk", coarse_vecs, residual, precision=highest)
        coarse_term = jnp.dot(restricted, coarse_factor, precision=highest)
        local_energy = jnp.sum(residual * own_part, axis=(0, 2))
        summed = all_sum(jnp.concatenate([coarse_term, local_energy[:, None]], axis=1))
        coarse_sum = summed[:, :-1]
        spread = jnp.einsum("lc,kc->lk", coarse_sum, coarse_factor, precision=highest)
        smoothed = own_part + jnp.einsum("kbi,lk->bli", coarse_vecs, spread, precision=highest)
        energy = summed[:, -1] + jnp.sum(coarse_sum * coarse_sum, axis=1)
        return (smoothed, energy)

    residual = load_vectors[0, 0]
    solution = jnp.zeros_like(residual)
    smoothed, energy = precondition(residual)
    direction = smoothed
    for iteration in range(ITERS):
        rounded = direction.astype(jnp.bfloat16)
        backward = -jnp.einsum("bsij,bli->bslj", weights, rounded, preferred_element_type=jnp.float32)
        partial_value = spread_terms(backward.reshape(BZ * NS, NLOAD * DOF), (NLOAD, DOF))
        ghosts, folded = exchange(rounded, partial_value.astype(jnp.bfloat16), partial_value[1, 1])
        padded = jnp.pad(ghosts, ((0, 0), (0, 0), (1, 1), (0, 0), (0, 0))).reshape(
            ghost_count, NLOAD, DOF
        )
        gathered = jnp.take(padded, col_codes, axis=0)
        forward = row_total[:, None, :] * rounded - jnp.einsum(
            "bsij,bslj->bli", weights, gathered, preferred_element_type=jnp.float32
        )
        folded = folded + column_fold[:, None, :] * rounded.astype(jnp.float32)
        diagonal = jnp.einsum(
            "bij,blj->bli", self_block, rounded, preferred_element_type=jnp.float32
        )
        operator_out = diagonal + forward + folded
        curve_sum = all_sum(jnp.sum(direction * operator_out, axis=(0, 2)), radix=4)
        step_scale = (energy / curve_sum)[None, :, None]
        solution = solution + step_scale * direction
        residual = residual - step_scale * operator_out
        if iteration + 1 < ITERS:
            smoothed, new_energy = precondition(residual)
            direction = smoothed + (new_energy / energy)[None, :, None] * direction
            energy = new_energy
    return (solution[None, None], residual[None, None])


def solution(mesh):
    in_specs = (
        P("gx", "gy", None, None, None),
        P("gx", "gy", None, None, None),
        P("gx", "gy", None, None, None, None),
        P("gx", "gy", None, None),
        P("gx", "gy", None, None),
        P("gx", "gy", None, None),
        P("gx", "gy", None, None, None),
        P(("gx", "gy"), None),
    )
    out_specs = (P("gx", "gy", None, None, None), P("gx", "gy", None, None, None))
    return jax.shard_map(
        per_device, mesh=mesh, in_specs=in_specs, out_specs=out_specs, check_vma=False
    )
```

```python
import jax
import jax.numpy as jnp
from jax import lax
from jax.sharding import PartitionSpec as P

COMP = 3
PB = 64
DOF = 192
NS = 13
BZ = 8
NLOAD = 8
ITERS = 2


highest = lax.Precision.HIGHEST


def all_sum(x, radix=2, riders=(), work=None):
    riders = list(riders)
    outs = []
    pending = None
    stage = 0
    for axis in ("gy", "gx"):
        size = lax.axis_size(axis)
        if size & (size - 1):
            x = lax.psum(x, axis)
            continue
        span = 1
        while span < size:
            count = min(radix, size // span)
            values = [x] + [
                lax.ppermute(x, axis, [(i, i ^ (o * span)) for i in range(size)])
                for o in range(1, count)
            ]
            width = 1
            while width < count:
                values = [
                    values[o] + values[o + width] if o % (2 * width) == 0 else None
                    for o in range(count)
                ]
                width *= 2
            x = values[0]
            span *= count
            if stage < len(riders):
                if pending is None:
                    x, rider = lax.optimization_barrier((x, riders[stage]))
                else:
                    x, pending, rider = lax.optimization_barrier((x, pending, riders[stage]))
                    outs.append(pending)
                pending = work(rider)
            stage += 1
    if riders:
        outs.append(pending)
        return x, outs
    return x


def shift_pairs(size):
    up = [(i, i + 1) for i in range(size - 1)]
    return up, [(j, i) for i, j in up]


def fold_in(part):
    up, down = shift_pairs(lax.axis_size("gx"))
    from_left = lax.ppermute(part[2], "gx", up)
    from_right = lax.ppermute(part[0], "gx", down)
    here_x = jnp.stack([from_left, part[1], from_right])
    up, down = shift_pairs(lax.axis_size("gy"))
    from_below = lax.ppermute(here_x[:, 2], "gy", up)
    from_above = lax.ppermute(here_x[:, 0], "gy", down)
    return jnp.sum(here_x[:, 1], axis=0) + jnp.sum(from_below, axis=0) + jnp.sum(from_above, axis=0)


def exchange(rounded, part, own_part):
    up, down = shift_pairs(lax.axis_size("gx"))
    from_left = lax.ppermute(jnp.concatenate([rounded[None], part[2]]), "gx", up)
    from_right = lax.ppermute(jnp.concatenate([rounded[None], part[0]]), "gx", down)
    ghost_x = jnp.stack([from_left[0], rounded, from_right[0]])
    part_x = jnp.stack([from_left[1:], part[1], from_right[1:]])
    up, down = shift_pairs(lax.axis_size("gy"))
    from_below = lax.ppermute(jnp.concatenate([ghost_x, part_x[:, 2]]), "gy", up)
    from_above = lax.ppermute(jnp.concatenate([ghost_x, part_x[:, 0]]), "gy", down)
    ghosts = jnp.stack([from_below[:3], ghost_x, from_above[:3]], axis=1)
    wide = jnp.float32
    folded = own_part + from_left[2].astype(wide) + from_right[2].astype(wide)
    folded = folded + jnp.sum(from_below[3:].astype(wide), axis=0)
    folded = folded + jnp.sum(from_above[3:].astype(wide), axis=0)
    return ghosts, folded


def unpack_bits(packed):
    shifts = jnp.arange(16, dtype=jnp.int32)
    bitset = jnp.right_shift(packed[..., None], shifts) & 1
    return bitset.reshape(packed.shape[:-1] + (packed.shape[-1] * 16,))


def masked_blocks(stiffness, packed):
    intact = unpack_bits(packed).astype(stiffness.dtype)
    leading = stiffness.shape[:-1]
    spread = (
        jnp.arange(DOF, dtype=jnp.int32)[:, None] % PB == jnp.arange(PB, dtype=jnp.int32)[None, :]
    ).astype(stiffness.dtype)
    wide = jnp.einsum("Ii,...ij,Jj->...IJ", spread, intact, spread, preferred_element_type=jnp.float32)
    return stiffness.reshape(leading + (DOF, DOF)) * wide.astype(stiffness.dtype)


def per_device(
    load_vectors,
    bond_stiffness,
    intact_words,
    block_cols,
    self_stiffness,
    block_inverse,
    coarse_basis,
    coarse_factor,
):
    col_codes = block_cols[0, 0]
    depth_span = BZ + 2
    ghost_count = 9 * depth_span
    selector = (
        jnp.arange(ghost_count, dtype=jnp.int32)[:, None] == col_codes.reshape(-1)[None, :]
    ).astype(jnp.bfloat16)
    self_block = self_stiffness[0, 0].reshape(BZ, DOF, DOF)
    inverse = block_inverse[0, 0].reshape(BZ, DOF, DOF)
    coarse_vecs = coarse_basis[0, 0]

    def spread_terms(flat_terms, tail):
        high_part = flat_terms.astype(jnp.bfloat16)
        low_part = (flat_terms - high_part.astype(jnp.float32)).astype(jnp.bfloat16)
        spread = jnp.dot(selector, high_part, preferred_element_type=jnp.float32) + jnp.dot(
            selector, low_part, preferred_element_type=jnp.float32
        )
        return spread.reshape((3, 3, depth_span) + tail)[:, :, 1 : depth_span - 1]


    def chunk_work(rider):
        piece = masked_blocks(*rider)
        return (
            piece,
            jnp.sum(piece, axis=(0, 2), dtype=jnp.float32),
            jnp.sum(piece, axis=1, dtype=jnp.float32),
        )

    def precondition(residual, riders=()):
        own_part = jnp.einsum("bij,blj->bli", inverse, residual, precision=highest)
        restricted = jnp.einsum("kbi,bli->lk", coarse_vecs, residual, precision=highest)
        coarse_term = jnp.dot(restricted, coarse_factor, precision=highest)
        local_energy = jnp.sum(residual * own_part, axis=(0, 2))
        summed = all_sum(jnp.concatenate([coarse_term, local_energy[:, None]], axis=1), riders=riders, work=chunk_work)
        if riders:
            summed, riders = summed
        coarse_sum = summed[:, :-1]
        spread = jnp.einsum("lc,kc->lk", coarse_sum, coarse_factor, precision=highest)
        smoothed = own_part + jnp.einsum("kbi,lk->bli", coarse_vecs, spread, precision=highest)
        energy = summed[:, -1] + jnp.sum(coarse_sum * coarse_sum, axis=1)
        return (smoothed, energy, riders)

    residual = load_vectors[0, 0]
    solution = jnp.zeros_like(residual)
    chunks = [(bond_stiffness[0, 0, b], intact_words[0, 0, b]) for b in range(BZ)]
    smoothed, energy, chunks = precondition(residual, chunks)
    direction = smoothed
    weights = jnp.stack([piece for piece, _, _ in chunks])
    row_total = jnp.stack([rows for _, rows, _ in chunks])
    column_total = jnp.stack([columns for _, _, columns in chunks])
    column_spread = spread_terms(column_total.reshape(BZ * NS, DOF), (DOF,))
    column_fold = fold_in(column_spread)
    for iteration in range(ITERS):
        rounded = direction.astype(jnp.bfloat16)
        backward = -jnp.einsum("bsij,bli->bslj", weights, rounded, preferred_element_type=jnp.float32)
        partial_value = spread_terms(backward.reshape(BZ * NS, NLOAD * DOF), (NLOAD, DOF))
        ghosts, folded = exchange(rounded, partial_value.astype(jnp.bfloat16), partial_value[1, 1])
        padded = jnp.pad(ghosts, ((0, 0), (0, 0), (1, 1), (0, 0), (0, 0))).reshape(
            ghost_count, NLOAD, DOF
        )
        gathered = jnp.take(padded, col_codes, axis=0)
        forward = row_total[:, None, :] * rounded - jnp.einsum(
            "bsij,bslj->bli", weights, gathered, preferred_element_type=jnp.float32
        )
        folded = folded + column_fold[:, None, :] * rounded.astype(jnp.float32)
        diagonal = jnp.einsum(
            "bij,blj->bli", self_block, rounded, preferred_element_type=jnp.float32
        )
        operator_out = diagonal + forward + folded
        curve_sum = all_sum(jnp.sum(direction * operator_out, axis=(0, 2)), radix=4)
        step_scale = (energy / curve_sum)[None, :, None]
        solution = solution + step_scale * direction
        residual = residual - step_scale * operator_out
        if iteration + 1 < ITERS:
            smoothed, new_energy, _ = precondition(residual)
            direction = smoothed + (new_energy / energy)[None, :, None] * direction
            energy = new_energy
    return (solution[None, None], residual[None, None])


def solution(mesh):
    in_specs = (
        P("gx", "gy", None, None, None),
        P("gx", "gy", None, None, None),
        P("gx", "gy", None, None, None, None),
        P("gx", "gy", None, None),
        P("gx", "gy", None, None),
        P("gx", "gy", None, None),
        P("gx", "gy", None, None, None),
        P(("gx", "gy"), None),
    )
    out_specs = (P("gx", "gy", None, None, None), P("gx", "gy", None, None, None))
    return jax.shard_map(
        per_device, mesh=mesh, in_specs=in_specs, out_specs=out_specs, check_vma=False
    )
```

```python
import jax
import jax.numpy as jnp
from jax import lax
from jax.sharding import PartitionSpec as P

COMP = 3
PB = 64
DOF = 192
NS = 13
BZ = 8
NLOAD = 8
ITERS = 2


highest = lax.Precision.HIGHEST


def all_sum(x, radix=2):
    for axis in ("gy", "gx"):
        size = lax.axis_size(axis)
        if size & (size - 1):
            x = lax.psum(x, axis)
            continue
        span = 1
        while span < size:
            count = min(radix, size // span)
            values = [x] + [
                lax.ppermute(x, axis, [(i, i ^ (o * span)) for i in range(size)])
                for o in range(1, count)
            ]
            width = 1
            while width < count:
                values = [
                    values[o] + values[o + width] if o % (2 * width) == 0 else None
                    for o in range(count)
                ]
                width *= 2
            x = values[0]
            span *= count
    return x


def shift_pairs(size):
    up = [(i, i + 1) for i in range(size - 1)]
    return up, [(j, i) for i, j in up]


def fold_in(part):
    up, down = shift_pairs(lax.axis_size("gx"))
    from_left = lax.ppermute(part[2], "gx", up)
    from_right = lax.ppermute(part[0], "gx", down)
    here_x = jnp.stack([from_left, part[1], from_right])
    up, down = shift_pairs(lax.axis_size("gy"))
    from_below = lax.ppermute(here_x[:, 2], "gy", up)
    from_above = lax.ppermute(here_x[:, 0], "gy", down)
    return jnp.sum(here_x[:, 1], axis=0) + jnp.sum(from_below, axis=0) + jnp.sum(from_above, axis=0)


def exchange(rounded, part, own_part):
    up, down = shift_pairs(lax.axis_size("gx"))
    from_left = lax.ppermute(jnp.concatenate([rounded[None], part[2]]), "gx", up)
    from_right = lax.ppermute(jnp.concatenate([rounded[None], part[0]]), "gx", down)
    ghost_x = jnp.stack([from_left[0], rounded, from_right[0]])
    part_x = jnp.stack([from_left[1:], part[1], from_right[1:]])
    up, down = shift_pairs(lax.axis_size("gy"))
    from_below = lax.ppermute(jnp.concatenate([ghost_x, part_x[:, 2]]), "gy", up)
    from_above = lax.ppermute(jnp.concatenate([ghost_x, part_x[:, 0]]), "gy", down)
    ghosts = jnp.stack([from_below[:3], ghost_x, from_above[:3]], axis=1)
    wide = jnp.float32
    folded = own_part + from_left[2].astype(wide) + from_right[2].astype(wide)
    folded = folded + jnp.sum(from_below[3:].astype(wide), axis=0)
    folded = folded + jnp.sum(from_above[3:].astype(wide), axis=0)
    return ghosts, folded


def unpack_bits(packed):
    shifts = jnp.arange(16, dtype=jnp.int32)
    bitset = jnp.right_shift(packed[..., None], shifts) & 1
    return bitset.reshape(packed.shape[:-1] + (packed.shape[-1] * 16,))


def masked_blocks(stiffness, packed):
    intact = unpack_bits(packed).astype(stiffness.dtype)
    leading = stiffness.shape[:-1]
    spread = (
        jnp.arange(DOF, dtype=jnp.int32)[:, None] % PB == jnp.arange(PB, dtype=jnp.int32)[None, :]
    ).astype(stiffness.dtype)
    wide = jnp.einsum("Ii,...ij,Jj->...IJ", spread, intact, spread, preferred_element_type=jnp.float32)
    return stiffness.reshape(leading + (DOF, DOF)) * wide.astype(stiffness.dtype)


def per_device(
    load_vectors,
    bond_stiffness,
    intact_words,
    block_cols,
    self_stiffness,
    block_inverse,
    coarse_basis,
    coarse_factor,
):
    weights = masked_blocks(bond_stiffness[0, 0], intact_words[0, 0])
    row_total = jnp.sum(weights, axis=(1, 3), dtype=jnp.float32)
    column_total = jnp.sum(weights, axis=2, dtype=jnp.float32)
    col_codes = block_cols[0, 0]
    depth_span = BZ + 2
    ghost_count = 9 * depth_span
    selector = (
        jnp.arange(ghost_count, dtype=jnp.int32)[:, None] == col_codes.reshape(-1)[None, :]
    ).astype(jnp.bfloat16)
    self_block = self_stiffness[0, 0].reshape(BZ, DOF, DOF)
    inverse = block_inverse[0, 0].reshape(BZ, DOF, DOF)
    coarse_vecs = coarse_basis[0, 0]

    def spread_terms(flat_terms, tail):
        high_part = flat_terms.astype(jnp.bfloat16)
        low_part = (flat_terms - high_part.astype(jnp.float32)).astype(jnp.bfloat16)
        spread = jnp.dot(selector, high_part, preferred_element_type=jnp.float32) + jnp.dot(
            selector, low_part, preferred_element_type=jnp.float32
        )
        return spread.reshape((3, 3, depth_span) + tail)[:, :, 1 : depth_span - 1]

    column_spread = spread_terms(column_total.reshape(BZ * NS, DOF), (DOF,))

    def precondition(residual):
        own_part = jnp.einsum("bij,blj->bli", inverse, residual, precision=highest)
        restricted = jnp.einsum("kbi,bli->lk", coarse_vecs, residual, precision=highest)
        coarse_term = jnp.dot(restricted, coarse_factor, precision=highest)
        local_energy = jnp.sum(residual * own_part, axis=(0, 2))
        summed = all_sum(jnp.concatenate([coarse_term, local_energy[:, None]], axis=1))
        coarse_sum = summed[:, :-1]
        spread = jnp.einsum("lc,kc->lk", coarse_sum, coarse_factor, precision=highest)
        smoothed = own_part + jnp.einsum("kbi,lk->bli", coarse_vecs, spread, precision=highest)
        energy = summed[:, -1] + jnp.sum(coarse_sum * coarse_sum, axis=1)
        return (smoothed, energy)

    residual = load_vectors[0, 0]
    solution = jnp.zeros_like(residual)
    smoothed, energy = precondition(residual)
    direction = smoothed
    for iteration in range(ITERS):
        rounded = direction.astype(jnp.bfloat16)
        if iteration == 0:
            rounded, column_spread = lax.optimization_barrier((rounded, column_spread))
            column_fold = fold_in(column_spread)
        backward = -jnp.einsum("bsij,bli->bslj", weights, rounded, preferred_element_type=jnp.float32)
        partial_value = spread_terms(backward.reshape(BZ * NS, NLOAD * DOF), (NLOAD, DOF))
        ghosts, folded = exchange(rounded, partial_value.astype(jnp.bfloat16), partial_value[1, 1])
        padded = jnp.pad(ghosts, ((0, 0), (0, 0), (1, 1), (0, 0), (0, 0))).reshape(
            ghost_count, NLOAD, DOF
        )
        gathered = jnp.take(padded, col_codes, axis=0)
        forward = row_total[:, None, :] * rounded - jnp.einsum(
            "bsij,bslj->bli", weights, gathered, preferred_element_type=jnp.float32
        )
        folded = folded + column_fold[:, None, :] * rounded.astype(jnp.float32)
        diagonal = jnp.einsum(
            "bij,blj->bli", self_block, rounded, preferred_element_type=jnp.float32
        )
        operator_out = diagonal + forward + folded
        curve_sum = all_sum(jnp.sum(direction * operator_out, axis=(0, 2)), radix=4)
        step_scale = (energy / curve_sum)[None, :, None]
        solution = solution + step_scale * direction
        residual = residual - step_scale * operator_out
        if iteration + 1 < ITERS:
            smoothed, new_energy = precondition(residual)
            direction = smoothed + (new_energy / energy)[None, :, None] * direction
            energy = new_energy
    return (solution[None, None], residual[None, None])


def solution(mesh):
    in_specs = (
        P("gx", "gy", None, None, None),
        P("gx", "gy", None, None, None),
        P("gx", "gy", None, None, None, None),
        P("gx", "gy", None, None),
        P("gx", "gy", None, None),
        P("gx", "gy", None, None),
        P("gx", "gy", None, None, None),
        P(("gx", "gy"), None),
    )
    out_specs = (P("gx", "gy", None, None, None), P("gx", "gy", None, None, None))
    return jax.shard_map(
        per_device, mesh=mesh, in_specs=in_specs, out_specs=out_specs, check_vma=False
    )
```

```python
import jax
import jax.numpy as jnp
from jax import lax
from jax.sharding import PartitionSpec as P

COMP = 3
PB = 64
DOF = 192
NS = 13
BZ = 8
NLOAD = 8
ITERS = 2


highest = lax.Precision.HIGHEST


def all_sum(x, radix=2):
    for axis in ("gy", "gx"):
        size = lax.axis_size(axis)
        if size & (size - 1):
            x = lax.psum(x, axis)
            continue
        span = 1
        while span < size:
            count = min(radix, size // span)
            values = [x] + [
                lax.ppermute(x, axis, [(i, i ^ (o * span)) for i in range(size)])
                for o in range(1, count)
            ]
            width = 1
            while width < count:
                values = [
                    values[o] + values[o + width] if o % (2 * width) == 0 else None
                    for o in range(count)
                ]
                width *= 2
            x = values[0]
            span *= count
    return x


def shift_pairs(size):
    up = [(i, i + 1) for i in range(size - 1)]
    return up, [(j, i) for i, j in up]


def fold_in(part):
    up, down = shift_pairs(lax.axis_size("gx"))
    from_left = lax.ppermute(part[2], "gx", up)
    from_right = lax.ppermute(part[0], "gx", down)
    here_x = jnp.stack([from_left, part[1], from_right])
    up, down = shift_pairs(lax.axis_size("gy"))
    from_below = lax.ppermute(here_x[:, 2], "gy", up)
    from_above = lax.ppermute(here_x[:, 0], "gy", down)
    return jnp.sum(here_x[:, 1], axis=0) + jnp.sum(from_below, axis=0) + jnp.sum(from_above, axis=0)


def exchange(rounded, part, own_part):
    up, down = shift_pairs(lax.axis_size("gx"))
    from_left = lax.ppermute(jnp.concatenate([rounded[None], part[2]]), "gx", up)
    from_right = lax.ppermute(jnp.concatenate([rounded[None], part[0]]), "gx", down)
    ghost_x = jnp.stack([from_left[0], rounded, from_right[0]])
    part_x = jnp.stack([from_left[1:], part[1], from_right[1:]])
    up, down = shift_pairs(lax.axis_size("gy"))
    from_below = lax.ppermute(jnp.concatenate([ghost_x, part_x[:, 2]]), "gy", up)
    from_above = lax.ppermute(jnp.concatenate([ghost_x, part_x[:, 0]]), "gy", down)
    ghosts = jnp.stack([from_below[:3], ghost_x, from_above[:3]], axis=1)
    wide = jnp.float32
    folded = own_part + from_left[2].astype(wide) + from_right[2].astype(wide)
    folded = folded + jnp.sum(from_below[3:].astype(wide), axis=0)
    folded = folded + jnp.sum(from_above[3:].astype(wide), axis=0)
    return ghosts, folded


def unpack_bits(packed):
    shifts = jnp.arange(16, dtype=jnp.int32)
    bitset = jnp.right_shift(packed[..., None], shifts) & 1
    return bitset.reshape(packed.shape[:-1] + (packed.shape[-1] * 16,))


def masked_blocks(stiffness, packed):
    intact = unpack_bits(packed).astype(stiffness.dtype)
    leading = stiffness.shape[:-1]
    spread = (
        jnp.arange(DOF, dtype=jnp.int32)[:, None] % PB == jnp.arange(PB, dtype=jnp.int32)[None, :]
    ).astype(stiffness.dtype)
    wide = jnp.einsum("Ii,...ij,Jj->...IJ", spread, intact, spread, preferred_element_type=jnp.float32)
    return stiffness.reshape(leading + (DOF, DOF)) * wide.astype(stiffness.dtype)


def per_device(
    load_vectors,
    bond_stiffness,
    intact_words,
    block_cols,
    self_stiffness,
    block_inverse,
    coarse_basis,
    coarse_factor,
):
    weights = masked_blocks(bond_stiffness[0, 0], intact_words[0, 0])
    row_total = jnp.sum(weights, axis=(1, 3), dtype=jnp.float32)
    column_total = jnp.sum(weights, axis=2, dtype=jnp.float32)
    col_codes = block_cols[0, 0]
    depth_span = BZ + 2
    ghost_count = 9 * depth_span
    selector = (
        jnp.arange(ghost_count, dtype=jnp.int32)[:, None] == col_codes.reshape(-1)[None, :]
    ).astype(jnp.bfloat16)
    self_block = self_stiffness[0, 0].reshape(BZ, DOF, DOF)
    inverse = block_inverse[0, 0].reshape(BZ, DOF, DOF)
    coarse_vecs = coarse_basis[0, 0]

    def spread_terms(flat_terms, tail):
        high_part = flat_terms.astype(jnp.bfloat16)
        low_part = (flat_terms - high_part.astype(jnp.float32)).astype(jnp.bfloat16)
        spread = jnp.dot(selector, high_part, preferred_element_type=jnp.float32) + jnp.dot(
            selector, low_part, preferred_element_type=jnp.float32
        )
        return spread.reshape((3, 3, depth_span) + tail)[:, :, 1 : depth_span - 1]

    column_spread = spread_terms(column_total.reshape(BZ * NS, DOF), (DOF,))
    column_fold = fold_in(column_spread)

    def precondition(residual):
        own_part = jnp.einsum("bij,blj->bli", inverse, residual, precision=highest)
        restricted = jnp.einsum("kbi,bli->lk", coarse_vecs, residual, precision=highest)
        coarse_term = jnp.dot(restricted, coarse_factor, precision=highest)
        local_energy = jnp.sum(residual * own_part, axis=(0, 2))
        summed = all_sum(jnp.concatenate([coarse_term, local_energy[:, None]], axis=1))
        coarse_sum = summed[:, :-1]
        spread = jnp.einsum("lc,kc->lk", coarse_sum, coarse_factor, precision=highest)
        smoothed = own_part + jnp.einsum("kbi,lk->bli", coarse_vecs, spread, precision=highest)
        energy = summed[:, -1] + jnp.sum(coarse_sum * coarse_sum, axis=1)
        return (smoothed, energy)

    residual = load_vectors[0, 0]
    solution = jnp.zeros_like(residual)
    smoothed, energy = precondition(residual)
    direction = smoothed
    for iteration in range(ITERS):
        rounded = direction.astype(jnp.bfloat16)
        backward = -jnp.einsum("bsij,bli->bslj", weights, rounded, preferred_element_type=jnp.float32)
        partial_value = spread_terms(backward.reshape(BZ * NS, NLOAD * DOF), (NLOAD, DOF))
        ghosts, folded = exchange(rounded, partial_value.astype(jnp.bfloat16), partial_value[1, 1])
        padded = jnp.pad(ghosts, ((0, 0), (0, 0), (1, 1), (0, 0), (0, 0))).reshape(
            ghost_count, NLOAD, DOF
        )
        gathered = jnp.take(padded, col_codes, axis=0)
        forward = row_total[:, None, :] * rounded - jnp.einsum(
            "bsij,bslj->bli", weights, gathered, preferred_element_type=jnp.float32
        )
        folded = folded + column_fold[:, None, :] * rounded.astype(jnp.float32)
        diagonal = jnp.einsum(
            "bij,blj->bli", self_block, rounded, preferred_element_type=jnp.float32
        )
        operator_out = diagonal + forward + folded
        curve_sum = all_sum(jnp.sum(direction * operator_out, axis=(0, 2)))
        step_scale = (energy / curve_sum)[None, :, None]
        solution = solution + step_scale * direction
        residual = residual - step_scale * operator_out
        if iteration + 1 < ITERS:
            smoothed, new_energy = precondition(residual)
            direction = smoothed + (new_energy / energy)[None, :, None] * direction
            energy = new_energy
    return (solution[None, None], residual[None, None])


def solution(mesh):
    in_specs = (
        P("gx", "gy", None, None, None),
        P("gx", "gy", None, None, None),
        P("gx", "gy", None, None, None, None),
        P("gx", "gy", None, None),
        P("gx", "gy", None, None),
        P("gx", "gy", None, None),
        P("gx", "gy", None, None, None),
        P(("gx", "gy"), None),
    )
    out_specs = (P("gx", "gy", None, None, None), P("gx", "gy", None, None, None))
    return jax.shard_map(
        per_device, mesh=mesh, in_specs=in_specs, out_specs=out_specs, check_vma=False
    )
```

```python
import jax
import jax.numpy as jnp
from jax import lax
from jax.sharding import PartitionSpec as P

COMP = 3
PB = 64
DOF = 192
NS = 13
BZ = 8
NLOAD = 8
ITERS = 2


highest = lax.Precision.HIGHEST


def all_sum(x, radix=2):
    for axis in ("gy", "gx"):
        size = lax.axis_size(axis)
        if size & (size - 1):
            x = lax.psum(x, axis)
            continue
        span = 1
        while span < size:
            count = min(radix, size // span)
            values = [x] + [
                lax.ppermute(x, axis, [(i, i ^ (o * span)) for i in range(size)])
                for o in range(1, count)
            ]
            width = 1
            while width < count:
                values = [
                    values[o] + values[o + width] if o % (2 * width) == 0 else None
                    for o in range(count)
                ]
                width *= 2
            x = values[0]
            span *= count
    return x


def shift_pairs(size):
    up = [(i, i + 1) for i in range(size - 1)]
    return up, [(j, i) for i, j in up]


def fold_in(part):
    up, down = shift_pairs(lax.axis_size("gx"))
    from_left = lax.ppermute(part[2], "gx", up)
    from_right = lax.ppermute(part[0], "gx", down)
    here_x = jnp.stack([from_left, part[1], from_right])
    up, down = shift_pairs(lax.axis_size("gy"))
    from_below = lax.ppermute(here_x[:, 2], "gy", up)
    from_above = lax.ppermute(here_x[:, 0], "gy", down)
    return jnp.sum(here_x[:, 1], axis=0) + jnp.sum(from_below, axis=0) + jnp.sum(from_above, axis=0)


def exchange(rounded, part, own_part):
    up, down = shift_pairs(lax.axis_size("gx"))
    from_left = lax.ppermute(jnp.concatenate([rounded[None], part[2]]), "gx", up)
    from_right = lax.ppermute(jnp.concatenate([rounded[None], part[0]]), "gx", down)
    ghost_x = jnp.stack([from_left[0], rounded, from_right[0]])
    part_x = jnp.stack([from_left[1:], part[1], from_right[1:]])
    up, down = shift_pairs(lax.axis_size("gy"))
    from_below = lax.ppermute(jnp.concatenate([ghost_x, part_x[:, 2]]), "gy", up)
    from_above = lax.ppermute(jnp.concatenate([ghost_x, part_x[:, 0]]), "gy", down)
    ghosts = jnp.stack([from_below[:3], ghost_x, from_above[:3]], axis=1)
    wide = jnp.float32
    folded = own_part + from_left[2].astype(wide) + from_right[2].astype(wide)
    folded = folded + jnp.sum(from_below[3:].astype(wide), axis=0)
    folded = folded + jnp.sum(from_above[3:].astype(wide), axis=0)
    return ghosts, folded


def unpack_bits(packed):
    shifts = jnp.arange(16, dtype=jnp.int32)
    bitset = jnp.right_shift(packed[..., None], shifts) & 1
    return bitset.reshape(packed.shape[:-1] + (packed.shape[-1] * 16,))


def masked_blocks(stiffness, packed):
    intact = unpack_bits(packed).astype(stiffness.dtype)
    leading = stiffness.shape[:-1]
    spread = (
        jnp.arange(DOF, dtype=jnp.int32)[:, None] % PB == jnp.arange(PB, dtype=jnp.int32)[None, :]
    ).astype(stiffness.dtype)
    wide = jnp.einsum("Ii,...ij,Jj->...IJ", spread, intact, spread, preferred_element_type=jnp.float32)
    return stiffness.reshape(leading + (DOF, DOF)) * wide.astype(stiffness.dtype)


def per_device(
    load_vectors,
    bond_stiffness,
    intact_words,
    block_cols,
    self_stiffness,
    block_inverse,
    coarse_basis,
    coarse_factor,
):
    weights = masked_blocks(bond_stiffness[0, 0], intact_words[0, 0])
    row_total = jnp.sum(weights, axis=(1, 3), dtype=jnp.float32)
    column_total = jnp.sum(weights, axis=2, dtype=jnp.float32)
    col_codes = block_cols[0, 0]
    depth_span = BZ + 2
    ghost_count = 9 * depth_span
    selector = (
        jnp.arange(ghost_count, dtype=jnp.int32)[:, None] == col_codes.reshape(-1)[None, :]
    ).astype(jnp.bfloat16)
    self_block = self_stiffness[0, 0].reshape(BZ, DOF, DOF)
    inverse = block_inverse[0, 0].reshape(BZ, DOF, DOF)
    coarse_vecs = coarse_basis[0, 0]

    def spread_terms(flat_terms, tail):
        high_part = flat_terms.astype(jnp.bfloat16)
        low_part = (flat_terms - high_part.astype(jnp.float32)).astype(jnp.bfloat16)
        spread = jnp.dot(selector, high_part, preferred_element_type=jnp.float32) + jnp.dot(
            selector, low_part, preferred_element_type=jnp.float32
        )
        return spread.reshape((3, 3, depth_span) + tail)[:, :, 1 : depth_span - 1]

    column_spread = spread_terms(column_total.reshape(BZ * NS, DOF), (DOF,))
    column_fold = fold_in(column_spread)

    def precondition(residual):
        own_part = jnp.einsum("bij,blj->bli", inverse, residual, precision=highest)
        restricted = jnp.einsum("kbi,bli->lk", coarse_vecs, residual, precision=highest)
        coarse_term = jnp.dot(restricted, coarse_factor, precision=highest)
        local_energy = jnp.sum(residual * own_part, axis=(0, 2))
        summed = all_sum(jnp.concatenate([coarse_term, local_energy[:, None]], axis=1), radix=4)
        coarse_sum = summed[:, :-1]
        spread = jnp.einsum("lc,kc->lk", coarse_sum, coarse_factor, precision=highest)
        smoothed = own_part + jnp.einsum("kbi,lk->bli", coarse_vecs, spread, precision=highest)
        energy = summed[:, -1] + jnp.sum(coarse_sum * coarse_sum, axis=1)
        return (smoothed, energy)

    residual = load_vectors[0, 0]
    solution = jnp.zeros_like(residual)
    smoothed, energy = precondition(residual)
    direction = smoothed
    for iteration in range(ITERS):
        rounded = direction.astype(jnp.bfloat16)
        backward = -jnp.einsum("bsij,bli->bslj", weights, rounded, preferred_element_type=jnp.float32)
        partial_value = spread_terms(backward.reshape(BZ * NS, NLOAD * DOF), (NLOAD, DOF))
        ghosts, folded = exchange(rounded, partial_value.astype(jnp.bfloat16), partial_value[1, 1])
        padded = jnp.pad(ghosts, ((0, 0), (0, 0), (1, 1), (0, 0), (0, 0))).reshape(
            ghost_count, NLOAD, DOF
        )
        gathered = jnp.take(padded, col_codes, axis=0)
        forward = row_total[:, None, :] * rounded - jnp.einsum(
            "bsij,bslj->bli", weights, gathered, preferred_element_type=jnp.float32
        )
        folded = folded + column_fold[:, None, :] * rounded.astype(jnp.float32)
        diagonal = jnp.einsum(
            "bij,blj->bli", self_block, rounded, preferred_element_type=jnp.float32
        )
        operator_out = diagonal + forward + folded
        curve_sum = all_sum(jnp.sum(direction * operator_out, axis=(0, 2)), radix=4)
        step_scale = (energy / curve_sum)[None, :, None]
        solution = solution + step_scale * direction
        residual = residual - step_scale * operator_out
        if iteration + 1 < ITERS:
            smoothed, new_energy = precondition(residual)
            direction = smoothed + (new_energy / energy)[None, :, None] * direction
            energy = new_energy
    return (solution[None, None], residual[None, None])


def solution(mesh):
    in_specs = (
        P("gx", "gy", None, None, None),
        P("gx", "gy", None, None, None),
        P("gx", "gy", None, None, None, None),
        P("gx", "gy", None, None),
        P("gx", "gy", None, None),
        P("gx", "gy", None, None),
        P("gx", "gy", None, None, None),
        P(("gx", "gy"), None),
    )
    out_specs = (P("gx", "gy", None, None, None), P("gx", "gy", None, None, None))
    return jax.shard_map(
        per_device, mesh=mesh, in_specs=in_specs, out_specs=out_specs, check_vma=False
    )
```

```python
import jax
import jax.numpy as jnp
from jax import lax
from jax.sharding import PartitionSpec as P

COMP = 3
PB = 64
DOF = 192
NS = 13
BZ = 8
NLOAD = 8
ITERS = 2


highest = lax.Precision.HIGHEST


def all_sum(x, radix=2):
    for axis in ("gx", "gy"):
        size = lax.axis_size(axis)
        if size & (size - 1):
            x = lax.psum(x, axis)
            continue
        span = 1
        while span < size:
            count = min(radix, size // span)
            values = [x] + [
                lax.ppermute(x, axis, [(i, i ^ (o * span)) for i in range(size)])
                for o in range(1, count)
            ]
            width = 1
            while width < count:
                values = [
                    values[o] + values[o + width] if o % (2 * width) == 0 else None
                    for o in range(count)
                ]
                width *= 2
            x = values[0]
            span *= count
    return x


def shift_pairs(size):
    up = [(i, i + 1) for i in range(size - 1)]
    return up, [(j, i) for i, j in up]


def fold_in(part):
    up, down = shift_pairs(lax.axis_size("gx"))
    from_left = lax.ppermute(part[2], "gx", up)
    from_right = lax.ppermute(part[0], "gx", down)
    here_x = jnp.stack([from_left, part[1], from_right])
    up, down = shift_pairs(lax.axis_size("gy"))
    from_below = lax.ppermute(here_x[:, 2], "gy", up)
    from_above = lax.ppermute(here_x[:, 0], "gy", down)
    return jnp.sum(here_x[:, 1], axis=0) + jnp.sum(from_below, axis=0) + jnp.sum(from_above, axis=0)


def exchange(rounded, part, own_part):
    up, down = shift_pairs(lax.axis_size("gx"))
    from_left = lax.ppermute(jnp.concatenate([rounded[None], part[2]]), "gx", up)
    from_right = lax.ppermute(jnp.concatenate([rounded[None], part[0]]), "gx", down)
    ghost_x = jnp.stack([from_left[0], rounded, from_right[0]])
    part_x = jnp.stack([from_left[1:], part[1], from_right[1:]])
    up, down = shift_pairs(lax.axis_size("gy"))
    from_below = lax.ppermute(jnp.concatenate([ghost_x, part_x[:, 2]]), "gy", up)
    from_above = lax.ppermute(jnp.concatenate([ghost_x, part_x[:, 0]]), "gy", down)
    ghosts = jnp.stack([from_below[:3], ghost_x, from_above[:3]], axis=1)
    wide = jnp.float32
    folded = own_part + from_left[2].astype(wide) + from_right[2].astype(wide)
    folded = folded + jnp.sum(from_below[3:].astype(wide), axis=0)
    folded = folded + jnp.sum(from_above[3:].astype(wide), axis=0)
    return ghosts, folded


def unpack_bits(packed):
    shifts = jnp.arange(16, dtype=jnp.int32)
    bitset = jnp.right_shift(packed[..., None], shifts) & 1
    return bitset.reshape(packed.shape[:-1] + (packed.shape[-1] * 16,))


def masked_blocks(stiffness, packed):
    intact = unpack_bits(packed).astype(stiffness.dtype)
    leading = stiffness.shape[:-1]
    spread = (
        jnp.arange(DOF, dtype=jnp.int32)[:, None] % PB == jnp.arange(PB, dtype=jnp.int32)[None, :]
    ).astype(stiffness.dtype)
    wide = jnp.einsum("Ii,...ij,Jj->...IJ", spread, intact, spread, preferred_element_type=jnp.float32)
    return stiffness.reshape(leading + (DOF, DOF)) * wide.astype(stiffness.dtype)


def per_device(
    load_vectors,
    bond_stiffness,
    intact_words,
    block_cols,
    self_stiffness,
    block_inverse,
    coarse_basis,
    coarse_factor,
):
    weights = masked_blocks(bond_stiffness[0, 0], intact_words[0, 0])
    row_total = jnp.sum(weights, axis=(1, 3), dtype=jnp.float32)
    column_total = jnp.sum(weights, axis=2, dtype=jnp.float32)
    col_codes = block_cols[0, 0]
    depth_span = BZ + 2
    ghost_count = 9 * depth_span
    selector = (
        jnp.arange(ghost_count, dtype=jnp.int32)[:, None] == col_codes.reshape(-1)[None, :]
    ).astype(jnp.bfloat16)
    self_block = self_stiffness[0, 0].reshape(BZ, DOF, DOF)
    inverse = block_inverse[0, 0].reshape(BZ, DOF, DOF)
    coarse_vecs = coarse_basis[0, 0]

    def spread_terms(flat_terms, tail):
        high_part = flat_terms.astype(jnp.bfloat16)
        low_part = (flat_terms - high_part.astype(jnp.float32)).astype(jnp.bfloat16)
        spread = jnp.dot(selector, high_part, preferred_element_type=jnp.float32) + jnp.dot(
            selector, low_part, preferred_element_type=jnp.float32
        )
        return spread.reshape((3, 3, depth_span) + tail)[:, :, 1 : depth_span - 1]

    column_spread = spread_terms(column_total.reshape(BZ * NS, DOF), (DOF,))
    column_fold = fold_in(column_spread)

    def precondition(residual):
        own_part = jnp.einsum("bij,blj->bli", inverse, residual, precision=highest)
        restricted = jnp.einsum("kbi,bli->lk", coarse_vecs, residual, precision=highest)
        coarse_term = jnp.dot(restricted, coarse_factor, precision=highest)
        local_energy = jnp.sum(residual * own_part, axis=(0, 2))
        summed = all_sum(jnp.concatenate([coarse_term, local_energy[:, None]], axis=1), radix=4)
        coarse_sum = summed[:, :-1]
        spread = jnp.einsum("lc,kc->lk", coarse_sum, coarse_factor, precision=highest)
        smoothed = own_part + jnp.einsum("kbi,lk->bli", coarse_vecs, spread, precision=highest)
        energy = summed[:, -1] + jnp.sum(coarse_sum * coarse_sum, axis=1)
        return (smoothed, energy)

    residual = load_vectors[0, 0]
    solution = jnp.zeros_like(residual)
    smoothed, energy = precondition(residual)
    direction = smoothed
    for iteration in range(ITERS):
        rounded = direction.astype(jnp.bfloat16)
        backward = -jnp.einsum("bsij,bli->bslj", weights, rounded, preferred_element_type=jnp.float32)
        partial_value = spread_terms(backward.reshape(BZ * NS, NLOAD * DOF), (NLOAD, DOF))
        ghosts, folded = exchange(rounded, partial_value.astype(jnp.bfloat16), partial_value[1, 1])
        padded = jnp.pad(ghosts, ((0, 0), (0, 0), (1, 1), (0, 0), (0, 0))).reshape(
            ghost_count, NLOAD, DOF
        )
        gathered = jnp.take(padded, col_codes, axis=0)
        forward = row_total[:, None, :] * rounded - jnp.einsum(
            "bsij,bslj->bli", weights, gathered, preferred_element_type=jnp.float32
        )
        folded = folded + column_fold[:, None, :] * rounded.astype(jnp.float32)
        diagonal = jnp.einsum(
            "bij,blj->bli", self_block, rounded, preferred_element_type=jnp.float32
        )
        operator_out = diagonal + forward + folded
        curve_sum = all_sum(jnp.sum(direction * operator_out, axis=(0, 2)), radix=4)
        step_scale = (energy / curve_sum)[None, :, None]
        solution = solution + step_scale * direction
        residual = residual - step_scale * operator_out
        if iteration + 1 < ITERS:
            smoothed, new_energy = precondition(residual)
            direction = smoothed + (new_energy / energy)[None, :, None] * direction
            energy = new_energy
    return (solution[None, None], residual[None, None])


def solution(mesh):
    in_specs = (
        P("gx", "gy", None, None, None),
        P("gx", "gy", None, None, None),
        P("gx", "gy", None, None, None, None),
        P("gx", "gy", None, None),
        P("gx", "gy", None, None),
        P("gx", "gy", None, None),
        P("gx", "gy", None, None, None),
        P(("gx", "gy"), None),
    )
    out_specs = (P("gx", "gy", None, None, None), P("gx", "gy", None, None, None))
    return jax.shard_map(
        per_device, mesh=mesh, in_specs=in_specs, out_specs=out_specs, check_vma=False
    )
```
